256 devices in a mesh: ctx: 16 (over z_lo, x), ch: 16 (over y, z_hi, core).
Axes of the slice: x: 4, y: 4, z: 8 (z_hi: 2, z_lo: 4; z = z_hi * 4 + z_lo), core: 2. Of those that a mesh axis runs over, the one named last changes fastest.
Arguments:
- tokens: bfloat16 [4096, 8192], P('ctx', 'ch'), may hold values from -6 to 6
- in_weight: bfloat16 [8192, 3, 8192], P('ctx', None, 'ch'), may hold values from -0.0625 to 0.0625
- short_filter: bfloat16 [3, 3, 8192], P(None, None, 'ch'), may hold values from -3 to 3
- decay_rate: float32 [8192, 16], P('ch'), may hold values from 1.2207031e-05 to 0.0333333333
- residue: float32 [8192, 16], P('ch'), may hold values from -0.12 to 0.12
- skip_gain: float32 [8192], P('ch'), may hold values from -4 to 4
Outputs:
- filtered: bfloat16 [4096, 8192], P('ctx', 'ch')
The draws below stay inside these ranges and needn't reach their ends.
All inputs are finite; a program needn't handle non-finite values.
Results may differ from the reference program's by a relative error of at most 0.007.
Values may be sent and summed in bfloat16 or wider, within the bound.
No kernel may reach another device: no remote copies, remote signals or barrier semaphores. Data moves between devices by JAX's collectives and lax.ppermute only.
A program may use at most 128 MiB of HBM per device.

```python
import jax
import jax.numpy as jnp
from jax import lax

D = 8192
MODES = 16
SHORT_K = 3
TOKENS = 4096


def draw_decay_rate(key, part):
    fast_log = jnp.log(1.0 / 30.0)
    slow_log = jnp.log(0.05 / TOKENS)
    spread = jax.random.uniform(key, (D, MODES), jnp.float32, slow_log, fast_log)
    return jnp.clip(jnp.exp(spread), 0.05 / TOKENS, 1.0 / 30.0).astype(jnp.float32)


def block_levels(stream_key, shape, cuts, smallest, largest):
    def one(position, blocks):
        draws = jax.random.uniform(jax.random.fold_in(jax.random.fold_in(stream_key, 6), position), (blocks,), jnp.float32, smallest / len(cuts), largest / len(cuts))
        return jnp.repeat(jnp.exp(draws), shape[position] // blocks).reshape((-1,) + (1,) * (len(shape) - position - 1))

    level = one(*cuts[0])
    for cut in cuts[1:]:
        level = level * one(*cut)
    return level


def normal_values(rng, dims, width, reach, cuts=(), held_as=jnp.bfloat16):
    values = jax.random.normal(rng, dims, jnp.float32) * width
    if len(cuts) > 0:
        values = block_levels(rng, dims, cuts, -0.22, 0.18) * values
    return jnp.clip(values, min=-reach, max=reach).astype(held_as)


def setup_inputs(seed: int = 0) -> dict:
    keys = jax.random.split(jax.random.key(seed), 7)
    return {
        "tokens": normal_values(keys[0], (TOKENS, D), 1.0, 6.0, ((0, 16), (1, 16))),
        "in_weight": normal_values(keys[1], (D, 3, D), D ** -0.5, 0.0625, ((0, 16), (2, 16))),
        "short_filter": normal_values(keys[2], (SHORT_K, 3, D), 0.6, 3.0, ((2, 16),)),
        "decay_rate": draw_decay_rate(jax.random.fold_in(keys[6], 71), 0),
        "residue": normal_values(keys[4], (D, MODES), 0.02, 0.12, ((0, 16),), jnp.float32),
        "skip_gain": normal_values(keys[5], (D,), 1.0, 4.0, ((0, 16),), jnp.float32),
    }


def reference(tokens, in_weight, short_filter, decay_rate, residue, skip_gain):
    flat_weight = in_weight.reshape(D, 3 * D)
    projected = jnp.dot(tokens, flat_weight, preferred_element_type=jnp.float32).astype(jnp.bfloat16)
    projected = projected.reshape(TOKENS, 3, D)
    prefix = jnp.zeros((SHORT_K - 1, 3, D), jnp.float32)
    padded = jnp.concatenate([prefix, projected.astype(jnp.float32)], axis=0)
    filter_taps = short_filter.astype(jnp.float32)
    featured = jnp.zeros((TOKENS, 3, D), jnp.float32)
    for shift_back in range(SHORT_K):
        begin = SHORT_K - 1 - shift_back
        featured = featured + filter_taps[shift_back][None] * padded[begin:begin + TOKENS]
    query_gate = featured[:, 0]
    gated_rows = (featured[:, 1] * featured[:, 2]).astype(jnp.bfloat16)
    gated_wide = gated_rows.astype(jnp.float32)
    decay_factor = jnp.exp(-decay_rate)

    def advance(mode_state, gated_row):
        mode_state = decay_factor * mode_state + gated_row[:, None]
        return mode_state, jnp.sum(residue * mode_state, axis=1)

    unused, convolved = lax.scan(advance, jnp.zeros((D, MODES), jnp.float32), gated_wide)
    long_mix = convolved + skip_gain[None, :] * gated_wide
    return (query_gate * long_mix).astype(jnp.bfloat16)
```

```python
import jax
import jax.numpy as jnp
import numpy as np
from jax import lax
from jax.sharding import Mesh, PartitionSpec as P

exact_mode = lax.Precision.HIGHEST
SEQ = ("zl", "x")


def from_behind(block, axis, distance):
    devices = range(lax.axis_size(axis))
    route = [(i - distance, i) for i in devices if i - distance in devices]
    return lax.ppermute(block, axis, route)


def folded_in_pairs(pieces, combine):
    while len(jax.tree.leaves(pieces)[0]) > 1:
        pieces = jax.vmap(combine)(
            *(jax.tree.map(lambda part: part[side::2], pieces) for side in (0, 1))
        )
    return jax.tree.map(lambda part: part[0], pieces)


def entering_2(value, axis, combine, identity):
    size, position = (lax.axis_size(axis), lax.axis_index(axis))
    passed = jnp.arange(size) < position

    def kept(part, zero, own):
        return jnp.where(
            passed.reshape(-1, *(1 for _ in own.shape)), part, jnp.asarray(zero, own.dtype)
        )

    pieces = jax.tree.map(lambda v: lax.all_gather(v, axis, axis=0, tiled=False), value)
    return folded_in_pairs(jax.tree.map(kept, pieces, identity, value), combine)


def local(tokens, in_weight, short_filter, decay_rate, residue, skip_gain):
    tok_rows = tokens.shape[0]
    width_local = in_weight.shape[2]
    mode_count = decay_rate.shape[1]
    gathered = lax.all_gather(tokens, "ch", axis=1, tiled=True)
    column = lax.all_to_all(gathered, "zl", 1, 0, tiled=True)
    portion = lax.all_gather(in_weight, "x", axis=0, tiled=True)
    flat_part = portion.reshape(portion.shape[0], 3 * width_local)
    partial = jnp.dot(column, flat_part, preferred_element_type=jnp.float32)
    projected = lax.psum_scatter(partial, "zl", scatter_dimension=0, tiled=True)
    streams = projected.astype(jnp.bfloat16).reshape(tok_rows, 3, width_local)
    tap_count = short_filter.shape[0]
    last_rows = streams[tok_rows - (tap_count - 1) :]
    before = from_behind(last_rows, SEQ, 1)
    padded = jnp.concatenate([before, streams], axis=0).astype(jnp.float32)
    filter_taps = short_filter.astype(jnp.float32)
    featured = jnp.zeros((tok_rows, 3, width_local), jnp.float32)
    for shift_back in range(tap_count):
        begin = tap_count - 1 - shift_back
        featured = featured + filter_taps[shift_back][None] * padded[begin : begin + tok_rows]
    query_gate = featured[:, 0]
    gated_rows = (featured[:, 1] * featured[:, 2]).astype(jnp.bfloat16)
    gated_wide = gated_rows.astype(jnp.float32)
    position = jnp.arange(tok_rows, dtype=jnp.float32)
    powers = jnp.exp(-decay_rate[None, :, :] * (tok_rows - 1.0 - position)[:, None, None])
    zero_state = jnp.zeros(decay_rate.shape, jnp.float32)
    local_state = jnp.einsum("jc,jcr->cr", gated_wide, powers, precision=exact_mode)
    block_decay = jnp.exp(-decay_rate * float(tok_rows))

    def compose(earlier, later):
        return (earlier[0] * later[0], earlier[1] * later[0] + later[1])

    unused, incoming = entering_2(
        (block_decay, local_state), SEQ, compose, (jnp.ones_like(block_decay), zero_state)
    )
    growth = jnp.exp(decay_rate[None, :, :] * position[:, None, None])
    scaled = (gated_wide[:, :, None] * growth).reshape(tok_rows, width_local * mode_count)
    lower_mask = (jnp.arange(tok_rows)[:, None] >= jnp.arange(tok_rows)[None, :]).astype(
        jnp.float32
    )
    running_sum = jnp.dot(lower_mask, scaled, precision=exact_mode).reshape(
        tok_rows, width_local, mode_count
    )
    shrink = jnp.exp(-decay_rate[None, :, :] * position[:, None, None])
    entering = (incoming * jnp.exp(-decay_rate))[None]
    convolved = jnp.sum(residue[None] * shrink * (running_sum + entering), axis=2)
    long_mix = convolved + skip_gain[None, :] * gated_wide
    return (query_gate * long_mix).astype(jnp.bfloat16)


def split_mesh(mesh):
    ctx, ch = mesh.shape["ctx"], mesh.shape["ch"]
    inner = 4 if ctx % 4 == 0 else 1
    devices = np.asarray(mesh.devices).reshape(ctx // inner, inner, ch)
    return Mesh(devices, ("zl", "x", "ch"))


def solution(mesh):
    fine = split_mesh(mesh)
    in_specs = (
        P(SEQ, "ch"),
        P(SEQ, None, "ch"),
        P(None, None, "ch"),
        P("ch", None),
        P("ch", None),
        P("ch"),
    )
    out_specs = P(SEQ, "ch")
    return jax.shard_map(local, mesh=fine, in_specs=in_specs, out_specs=out_specs, check_vma=False)
```

```python
import jax
import jax.numpy as jnp
import numpy as np
from jax import lax
from jax.sharding import Mesh, PartitionSpec as P

exact_mode = lax.Precision.HIGHEST
SEQ = ("zl", "x")


def from_behind(block, axis, distance):
    devices = range(lax.axis_size(axis))
    route = [(i - distance, i) for i in devices if i - distance in devices]
    return lax.ppermute(block, axis, route)


def ring_sends(pieces, axis, size):
    position = lax.axis_index(axis)
    received = []
    for k in range(1, size):
        route = [(i, (i + k) % size) for i in range(size)]
        received.append(lax.ppermute(pieces(k, position), axis, route))
    return received


def local(tokens, in_weight, short_filter, decay_rate, residue, skip_gain):
    tok_rows = tokens.shape[0]
    width_local = in_weight.shape[2]
    mode_count = decay_rate.shape[1]
    feat_block = in_weight.shape[0]
    across, down = lax.axis_size("x"), lax.axis_size("zl")
    me_x, me_z = lax.axis_index("x"), lax.axis_index("zl")
    flat_own = in_weight.reshape(feat_block, 3 * width_local)
    weights = [flat_own] + ring_sends(lambda k, p: flat_own, "x", across)
    gathered = lax.all_gather(tokens, "ch", axis=1, tiled=True)
    chunk = gathered.shape[1] // down

    def chunk_for(k, p):
        return lax.dynamic_slice_in_dim(gathered, ((p + k) % down) * chunk, chunk, axis=1)

    rows = [chunk_for(0, me_z)] + ring_sends(chunk_for, "zl", down)
    column = jnp.concatenate(rows, axis=0)
    partial = jnp.zeros((column.shape[0], 3 * width_local), jnp.float32)
    for k in range(across):
        source = (me_x - k) % across
        taken = lax.dynamic_slice_in_dim(column, source * feat_block, feat_block, axis=1)
        partial = partial + jnp.dot(taken, weights[k], preferred_element_type=jnp.float32)
    pieces = partial.reshape(down, tok_rows, 3 * width_local)
    projected = pieces[0]
    for k in range(1, down):
        route = [(i, (i - k) % down) for i in range(down)]
        back = lax.ppermute(pieces[k].astype(jnp.bfloat16), "zl", route)
        projected = projected + back.astype(jnp.float32)
    streams = projected.astype(jnp.bfloat16).reshape(tok_rows, 3, width_local)
    tap_count = short_filter.shape[0]
    last_rows = streams[tok_rows - (tap_count - 1) :]
    before = from_behind(last_rows, SEQ, 1)
    padded = jnp.concatenate([before, streams], axis=0).astype(jnp.float32)
    filter_taps = short_filter.astype(jnp.float32)
    featured = jnp.zeros((tok_rows, 3, width_local), jnp.float32)
    for shift_back in range(tap_count):
        begin = tap_count - 1 - shift_back
        featured = featured + filter_taps[shift_back][None] * padded[begin : begin + tok_rows]
    query_gate = featured[:, 0]
    gated_rows = (featured[:, 1] * featured[:, 2]).astype(jnp.bfloat16)
    gated_wide = gated_rows.astype(jnp.float32)
    position = jnp.arange(tok_rows, dtype=jnp.float32)
    powers = jnp.exp(-decay_rate[None, :, :] * (tok_rows - 1.0 - position)[:, None, None])
    local_state = jnp.einsum("jc,jcr->cr", gated_wide, powers, precision=exact_mode)
    along = [local_state] + ring_sends(lambda k, p: local_state, "x", across)
    row = jnp.stack(along)
    states = jnp.stack([row] + ring_sends(lambda k, p: row, "zl", down))
    step_z = jnp.arange(down)[:, None]
    step_x = jnp.arange(across)[None, :]
    source = ((me_z - step_z) % down) * across + (me_x - step_x) % across
    lag = (me_z * across + me_x - 1 - source).astype(jnp.float32)
    decay_b = decay_rate[None, None]
    weight = jnp.exp(-decay_b * (float(tok_rows) * jnp.maximum(lag, 0.0))[:, :, None, None])
    weight = jnp.where((lag >= 0)[:, :, None, None], weight, 0.0)
    incoming = jnp.sum(weight * states, axis=(0, 1))
    growth = jnp.exp(decay_rate[None, :, :] * position[:, None, None])
    scaled = (gated_wide[:, :, None] * growth).reshape(tok_rows, width_local * mode_count)
    lower_mask = (jnp.arange(tok_rows)[:, None] >= jnp.arange(tok_rows)[None, :]).astype(
        jnp.float32
    )
    running_sum = jnp.dot(lower_mask, scaled, precision=exact_mode).reshape(
        tok_rows, width_local, mode_count
    )
    shrink = jnp.exp(-decay_rate[None, :, :] * position[:, None, None])
    entering = (incoming * jnp.exp(-decay_rate))[None]
    convolved = jnp.sum(residue[None] * shrink * (running_sum + entering), axis=2)
    long_mix = convolved + skip_gain[None, :] * gated_wide
    return (query_gate * long_mix).astype(jnp.bfloat16)


def split_mesh(mesh):
    ctx, ch = mesh.shape["ctx"], mesh.shape["ch"]
    inner = 4 if ctx % 4 == 0 else 1
    devices = np.asarray(mesh.devices).reshape(ctx // inner, inner, ch)
    return Mesh(devices, ("zl", "x", "ch"))


def solution(mesh):
    fine = split_mesh(mesh)
    in_specs = (
        P(SEQ, "ch"),
        P(SEQ, None, "ch"),
        P(None, None, "ch"),
        P("ch", None),
        P("ch", None),
        P("ch"),
    )
    out_specs = P(SEQ, "ch")
    return jax.shard_map(local, mesh=fine, in_specs=in_specs, out_specs=out_specs, check_vma=False)
```

```python
import jax
import jax.numpy as jnp
import numpy as np
from jax import lax
from jax.sharding import Mesh, PartitionSpec as P

exact_mode = lax.Precision.HIGHEST
SEQ = ("zl", "x")


def from_behind(block, axis, distance):
    devices = range(lax.axis_size(axis))
    route = [(i - distance, i) for i in devices if i - distance in devices]
    return lax.ppermute(block, axis, route)


def ring_sends(pieces, axis, size):
    position = lax.axis_index(axis)
    received = []
    for k in range(1, size):
        route = [(i, (i + k) % size) for i in range(size)]
        received.append(lax.ppermute(pieces(k, position), axis, route))
    return received


def block(tokens, in_weight, short_filter, decay_rate, residue, skip_gain):
    tok_rows = tokens.shape[0]
    width_local = in_weight.shape[2]
    mode_count = decay_rate.shape[1]
    feat_block = in_weight.shape[0]
    across, down = lax.axis_size("x"), lax.axis_size("zl")
    me_x, me_z = lax.axis_index("x"), lax.axis_index("zl")
    flat_own = in_weight.reshape(feat_block, 3 * width_local)
    weights = [flat_own] + ring_sends(lambda k, p: flat_own, "zl", down)
    gathered = lax.all_gather(tokens, "ch", axis=1, tiled=True)
    blocks = gathered.reshape(tok_rows, -1, across, feat_block)

    def chunk_for(k, p):
        part = lax.dynamic_index_in_dim(blocks, (p + k) % across, axis=2, keepdims=False)
        return part.reshape(tok_rows, -1)

    rows = [chunk_for(0, me_x)] + ring_sends(chunk_for, "x", across)
    column = jnp.concatenate(rows, axis=0)
    partial = jnp.zeros((column.shape[0], 3 * width_local), jnp.float32)
    for k in range(down):
        source = (me_z - k) % down
        taken = lax.dynamic_slice_in_dim(column, source * feat_block, feat_block, axis=1)
        partial = partial + jnp.dot(taken, weights[k], preferred_element_type=jnp.float32)
    pieces = partial.reshape(across, tok_rows, 3 * width_local)
    projected = pieces[0]
    for k in range(1, across):
        route = [(i, (i - k) % across) for i in range(across)]
        projected = projected + lax.ppermute(pieces[k], "x", route)
    streams = projected.astype(jnp.bfloat16).reshape(tok_rows, 3, width_local)
    tap_count = short_filter.shape[0]
    last_rows = streams[tok_rows - (tap_count - 1) :]
    before = from_behind(last_rows, SEQ, 1)
    padded = jnp.concatenate([before, streams], axis=0).astype(jnp.float32)
    filter_taps = short_filter.astype(jnp.float32)
    featured = jnp.zeros((tok_rows, 3, width_local), jnp.float32)
    for shift_back in range(tap_count):
        begin = tap_count - 1 - shift_back
        featured = featured + filter_taps[shift_back][None] * padded[begin : begin + tok_rows]
    query_gate = featured[:, 0]
    gated_rows = (featured[:, 1] * featured[:, 2]).astype(jnp.bfloat16)
    gated_wide = gated_rows.astype(jnp.float32)
    position = jnp.arange(tok_rows, dtype=jnp.float32)
    powers = jnp.exp(-decay_rate[None, :, :] * (tok_rows - 1.0 - position)[:, None, None])
    local_state = jnp.einsum("jc,jcr->cr", gated_wide, powers, precision=exact_mode)
    along = [local_state] + ring_sends(lambda k, p: local_state, "x", across)
    row = jnp.stack(along)
    states = jnp.stack([row] + ring_sends(lambda k, p: row, "zl", down))
    step_z = jnp.arange(down)[:, None]
    step_x = jnp.arange(across)[None, :]
    source = ((me_z - step_z) % down) * across + (me_x - step_x) % across
    lag = (me_z * across + me_x - 1 - source).astype(jnp.float32)
    decay_b = decay_rate[None, None]
    weight = jnp.exp(-decay_b * (float(tok_rows) * jnp.maximum(lag, 0.0))[:, :, None, None])
    weight = jnp.where((lag >= 0)[:, :, None, None], weight, 0.0)
    incoming = jnp.sum(weight * states, axis=(0, 1))
    growth = jnp.exp(decay_rate[None, :, :] * position[:, None, None])
    scaled = (gated_wide[:, :, None] * growth).reshape(tok_rows, width_local * mode_count)
    lower_mask = (jnp.arange(tok_rows)[:, None] >= jnp.arange(tok_rows)[None, :]).astype(
        jnp.float32
    )
    running_sum = jnp.dot(lower_mask, scaled, precision=exact_mode).reshape(
        tok_rows, width_local, mode_count
    )
    shrink = jnp.exp(-decay_rate[None, :, :] * position[:, None, None])
    entering = (incoming * jnp.exp(-decay_rate))[None]
    convolved = jnp.sum(residue[None] * shrink * (running_sum + entering), axis=2)
    long_mix = convolved + skip_gain[None, :] * gated_wide
    return (query_gate * long_mix).astype(jnp.bfloat16)


def split_mesh(mesh):
    ctx, ch = mesh.shape["ctx"], mesh.shape["ch"]
    inner = 4 if ctx % 4 == 0 else 1
    devices = np.asarray(mesh.devices).reshape(ctx // inner, inner, ch)
    return Mesh(devices, ("zl", "x", "ch"))


def solution(mesh):
    fine = split_mesh(mesh)
    in_specs = (
        P(SEQ, "ch"),
        P(SEQ, None, "ch"),
        P(None, None, "ch"),
        P("ch", None),
        P("ch", None),
        P("ch"),
    )
    out_specs = P(SEQ, "ch")
    return jax.shard_map(block, mesh=fine, in_specs=in_specs, out_specs=out_specs, check_vma=False)
```

```python
import jax
import jax.numpy as jnp
import numpy as np
from jax import lax
from jax.sharding import Mesh, PartitionSpec as P

exact_mode = lax.Precision.HIGHEST
SEQ = ("zl", "x")
SUB = ("zh", "c")
CH = ("y", "zh", "c")


def from_behind(block, axis, distance):
    devices = range(lax.axis_size(axis))
    route = [(i - distance, i) for i in devices if i - distance in devices]
    return lax.ppermute(block, axis, route)


def ring_sends(pieces, axis, size):
    position = lax.axis_index(axis)
    received = []
    for k in range(1, size):
        route = [(i, (i + k) % size) for i in range(size)]
        received.append(lax.ppermute(pieces(k, position), axis, route))
    return received


def block(tokens, in_weight, short_filter, decay_rate, residue, skip_gain):
    tok_rows = tokens.shape[0]
    width_local = in_weight.shape[2]
    mode_count = decay_rate.shape[1]
    feat_block = in_weight.shape[0]
    across, down = lax.axis_size("x"), lax.axis_size("zl")
    me_x, me_z = lax.axis_index("x"), lax.axis_index("zl")
    flat_own = in_weight.reshape(feat_block, 3 * width_local)
    weights = [flat_own] + ring_sends(lambda k, p: flat_own, "zl", down)
    swap = [(a * across + b, b * across + a) for a in range(across) for b in range(across)]
    moved = lax.ppermute(tokens, ("x",) + SUB, swap)
    gathered = lax.all_gather(moved, CH, axis=1, tiled=True)
    blocks = gathered.reshape(tok_rows, -1, across, feat_block)
    partial = jnp.zeros((across, tok_rows, 3 * width_local), jnp.float32)
    for k in range(down):
        source = (me_z - k) % down
        taken = lax.dynamic_index_in_dim(blocks, source, axis=1, keepdims=False)
        partial = partial + jnp.einsum(
            "rtu,uc->trc", taken, weights[k], preferred_element_type=jnp.float32
        )
    projected = lax.dynamic_index_in_dim(partial, me_x, axis=0, keepdims=False)
    for k in range(1, across):
        route = [(i, (i + k) % across) for i in range(across)]
        piece = lax.dynamic_index_in_dim(partial, (me_x + k) % across, axis=0, keepdims=False)
        projected = projected + lax.ppermute(piece, "x", route)
    streams = projected.astype(jnp.bfloat16).reshape(tok_rows, 3, width_local)
    tap_count = short_filter.shape[0]
    last_rows = streams[tok_rows - (tap_count - 1) :]
    before = from_behind(last_rows, SEQ, 1)
    padded = jnp.concatenate([before, streams], axis=0).astype(jnp.float32)
    filter_taps = short_filter.astype(jnp.float32)
    featured = jnp.zeros((tok_rows, 3, width_local), jnp.float32)
    for shift_back in range(tap_count):
        begin = tap_count - 1 - shift_back
        featured = featured + filter_taps[shift_back][None] * padded[begin : begin + tok_rows]
    query_gate = featured[:, 0]
    gated_rows = (featured[:, 1] * featured[:, 2]).astype(jnp.bfloat16)
    gated_wide = gated_rows.astype(jnp.float32)
    position = jnp.arange(tok_rows, dtype=jnp.float32)
    powers = jnp.exp(-decay_rate[None, :, :] * (tok_rows - 1.0 - position)[:, None, None])
    local_state = jnp.einsum("jc,jcr->cr", gated_wide, powers, precision=exact_mode)
    along = [local_state] + ring_sends(lambda k, p: local_state, "x", across)
    row = jnp.stack(along)
    states = jnp.stack([row] + ring_sends(lambda k, p: row, "zl", down))
    step_z = jnp.arange(down)[:, None]
    step_x = jnp.arange(across)[None, :]
    source = ((me_z - step_z) % down) * across + (me_x - step_x) % across
    lag = (me_z * across + me_x - 1 - source).astype(jnp.float32)
    decay_b = decay_rate[None, None]
    weight = jnp.exp(-decay_b * (float(tok_rows) * jnp.maximum(lag, 0.0))[:, :, None, None])
    weight = jnp.where((lag >= 0)[:, :, None, None], weight, 0.0)
    incoming = jnp.sum(weight * states, axis=(0, 1))
    growth = jnp.exp(decay_rate[None, :, :] * position[:, None, None])
    scaled = (gated_wide[:, :, None] * growth).reshape(tok_rows, width_local * mode_count)
    lower_mask = (jnp.arange(tok_rows)[:, None] >= jnp.arange(tok_rows)[None, :]).astype(
        jnp.float32
    )
    running_sum = jnp.dot(lower_mask, scaled, precision=exact_mode).reshape(
        tok_rows, width_local, mode_count
    )
    shrink = jnp.exp(-decay_rate[None, :, :] * position[:, None, None])
    entering = (incoming * jnp.exp(-decay_rate))[None]
    convolved = jnp.sum(residue[None] * shrink * (running_sum + entering), axis=2)
    long_mix = convolved + skip_gain[None, :] * gated_wide
    return (query_gate * long_mix).astype(jnp.bfloat16)


def split_mesh(mesh):
    ctx, ch = mesh.shape["ctx"], mesh.shape["ch"]
    devices = np.asarray(mesh.devices).reshape(ctx // 4, 4, ch // 4, 2, 2)
    return Mesh(devices, SEQ + CH)


def solution(mesh):
    fine = split_mesh(mesh)
    in_specs = (
        P(SEQ, CH),
        P(SEQ, None, CH),
        P(None, None, CH),
        P(CH, None),
        P(CH, None),
        P(CH),
    )
    out_specs = P(SEQ, CH)
    return jax.shard_map(block, mesh=fine, in_specs=in_specs, out_specs=out_specs, check_vma=False)
```

```python
import jax
import jax.numpy as jnp
import numpy as np
from jax import lax
from jax.sharding import Mesh, PartitionSpec as P

exact_mode = lax.Precision.HIGHEST
SEQ = ("zl", "x")
SUB = ("zh", "c")
CH = ("y", "zh", "c")


def from_behind(block, axis, distance):
    devices = range(lax.axis_size(axis))
    route = [(i - distance, i) for i in devices if i - distance in devices]
    return lax.ppermute(block, axis, route)


def ring_sends(pieces, axis, size):
    position = lax.axis_index(axis)
    received = []
    for k in range(1, size):
        route = [(i, (i + k) % size) for i in range(size)]
        received.append(lax.ppermute(pieces(k, position), axis, route))
    return received


def block(tokens, in_weight, short_filter, decay_rate, residue, skip_gain):
    tok_rows = tokens.shape[0]
    width_local = in_weight.shape[2]
    mode_count = decay_rate.shape[1]
    feat_block = in_weight.shape[0]
    across, down = lax.axis_size("x"), lax.axis_size("zl")
    me_x, me_z = lax.axis_index("x"), lax.axis_index("zl")
    flat_own = in_weight.reshape(feat_block, 3 * width_local)
    weights = [flat_own] + ring_sends(lambda k, p: flat_own, "zl", down)
    halves = lax.axis_size("zh")
    pair = lax.axis_size("c")
    me_h = lax.axis_index("zh")
    swap = [(a * across + b, b * across + a) for a in range(across) for b in range(across)]
    cross = [
        (a * across + b, b * across + ((a // pair + 1) % halves) * pair + a % pair)
        for a in range(across)
        for b in range(across)
    ]
    near = lax.ppermute(tokens, ("x",) + SUB, swap)
    far = lax.ppermute(tokens, ("x",) + SUB, cross)
    both = jnp.stack([jnp.where(me_h == 0, near, far), jnp.where(me_h == 0, far, near)])
    gathered = lax.all_gather(both, ("y", "c"), axis=0, tiled=False)
    blocks = gathered.reshape(-1, pair, halves, tok_rows, feat_block)
    partial = jnp.zeros((halves, pair, tok_rows, 3 * width_local), jnp.float32)
    for k in range(down):
        source = (me_z - k) % down
        taken = lax.dynamic_index_in_dim(blocks, source, axis=0, keepdims=False)
        partial = partial + jnp.einsum(
            "chru,uk->hcrk", taken, weights[k], preferred_element_type=jnp.float32
        )
    partial = partial.reshape(across, tok_rows, 3 * width_local)
    projected = lax.dynamic_index_in_dim(partial, me_x, axis=0, keepdims=False)
    for k in range(1, across):
        route = [(i, (i + k) % across) for i in range(across)]
        piece = lax.dynamic_index_in_dim(partial, (me_x + k) % across, axis=0, keepdims=False)
        projected = projected + lax.ppermute(piece, "x", route)
    streams = projected.astype(jnp.bfloat16).reshape(tok_rows, 3, width_local)
    tap_count = short_filter.shape[0]
    last_rows = streams[tok_rows - (tap_count - 1) :]
    before = from_behind(last_rows, SEQ, 1)
    padded = jnp.concatenate([before, streams], axis=0).astype(jnp.float32)
    filter_taps = short_filter.astype(jnp.float32)
    featured = jnp.zeros((tok_rows, 3, width_local), jnp.float32)
    for shift_back in range(tap_count):
        begin = tap_count - 1 - shift_back
        featured = featured + filter_taps[shift_back][None] * padded[begin : begin + tok_rows]
    query_gate = featured[:, 0]
    gated_rows = (featured[:, 1] * featured[:, 2]).astype(jnp.bfloat16)
    gated_wide = gated_rows.astype(jnp.float32)
    position = jnp.arange(tok_rows, dtype=jnp.float32)
    powers = jnp.exp(-decay_rate[None, :, :] * (tok_rows - 1.0 - position)[:, None, None])
    local_state = jnp.einsum("jc,jcr->cr", gated_wide, powers, precision=exact_mode)
    along = [local_state] + ring_sends(lambda k, p: local_state, "x", across)
    row = jnp.stack(along)
    states = jnp.stack([row] + ring_sends(lambda k, p: row, "zl", down))
    step_z = jnp.arange(down)[:, None]
    step_x = jnp.arange(across)[None, :]
    source = ((me_z - step_z) % down) * across + (me_x - step_x) % across
    lag = (me_z * across + me_x - 1 - source).astype(jnp.float32)
    decay_b = decay_rate[None, None]
    weight = jnp.exp(-decay_b * (float(tok_rows) * jnp.maximum(lag, 0.0))[:, :, None, None])
    weight = jnp.where((lag >= 0)[:, :, None, None], weight, 0.0)
    incoming = jnp.sum(weight * states, axis=(0, 1))
    growth = jnp.exp(decay_rate[None, :, :] * position[:, None, None])
    scaled = (gated_wide[:, :, None] * growth).reshape(tok_rows, width_local * mode_count)
    lower_mask = (jnp.arange(tok_rows)[:, None] >= jnp.arange(tok_rows)[None, :]).astype(
        jnp.float32
    )
    running_sum = jnp.dot(lower_mask, scaled, precision=exact_mode).reshape(
        tok_rows, width_local, mode_count
    )
    shrink = jnp.exp(-decay_rate[None, :, :] * position[:, None, None])
    entering = (incoming * jnp.exp(-decay_rate))[None]
    convolved = jnp.sum(residue[None] * shrink * (running_sum + entering), axis=2)
    long_mix = convolved + skip_gain[None, :] * gated_wide
    return (query_gate * long_mix).astype(jnp.bfloat16)


def split_mesh(mesh):
    ctx, ch = mesh.shape["ctx"], mesh.shape["ch"]
    devices = np.asarray(mesh.devices).reshape(ctx // 4, 4, ch // 4, 2, 2)
    return Mesh(devices, SEQ + CH)


def solution(mesh):
    fine = split_mesh(mesh)
    in_specs = (
        P(SEQ, CH),
        P(SEQ, None, CH),
        P(None, None, CH),
        P(CH, None),
        P(CH, None),
        P(CH),
    )
    out_specs = P(SEQ, CH)
    return jax.shard_map(block, mesh=fine, in_specs=in_specs, out_specs=out_specs, check_vma=False)
```

```python
import jax
import jax.numpy as jnp
import numpy as np
from jax import lax
from jax.sharding import Mesh, PartitionSpec as P

exact_mode = lax.Precision.HIGHEST
SEQ = ("zl", "x")
SUB = ("zh", "c")
CH = ("y", "zh", "c")


def from_behind(block, axis, distance):
    devices = range(lax.axis_size(axis))
    route = [(i - distance, i) for i in devices if i - distance in devices]
    return lax.ppermute(block, axis, route)


def ring_sends(pieces, axis, size):
    position = lax.axis_index(axis)
    received = []
    for k in range(1, size):
        route = [(i, (i + k) % size) for i in range(size)]
        received.append(lax.ppermute(pieces(k, position), axis, route))
    return received


def line_gather(piece, axis, size):
    below, above = [], []
    near_b = lax.ppermute(piece, axis, [(i, i + 1) for i in range(size - 1)])
    near_a = lax.ppermute(piece, axis, [(i + 1, i) for i in range(size - 1)])
    below.append(near_b)
    above.append(near_a)
    for d in range(2, size):
        near_b = lax.ppermute(near_b, axis, [(i, i + 1) for i in range(d - 1, size - 1)])
        near_a = lax.ppermute(near_a, axis, [(i + 1, i) for i in range(0, size - d)])
        below.append(near_b)
        above.append(near_a)
    return below, above


def block(tokens, in_weight, short_filter, decay_rate, residue, skip_gain):
    tok_rows = tokens.shape[0]
    width_local = in_weight.shape[2]
    mode_count = decay_rate.shape[1]
    feat_block = in_weight.shape[0]
    across, down = lax.axis_size("x"), lax.axis_size("zl")
    me_x, me_z = lax.axis_index("x"), lax.axis_index("zl")
    flat_own = in_weight.reshape(feat_block, 3 * width_local)
    below, above = line_gather(flat_own, "zl", down)
    halves = lax.axis_size("zh")
    pair = lax.axis_size("c")
    me_h = lax.axis_index("zh")
    swap = [(a * across + b, b * across + a) for a in range(across) for b in range(across)]
    cross = [
        (a * across + b, b * across + ((a // pair + 1) % halves) * pair + a % pair)
        for a in range(across)
        for b in range(across)
    ]
    near = lax.ppermute(tokens, ("x",) + SUB, swap)
    far = lax.ppermute(tokens, ("x",) + SUB, cross)
    both = jnp.stack([jnp.where(me_h == 0, near, far), jnp.where(me_h == 0, far, near)])
    gathered = lax.all_gather(both, ("y", "c"), axis=0, tiled=False)
    blocks = gathered.reshape(-1, pair, halves, tok_rows, feat_block)
    def contribution(source, weight):
        taken = lax.dynamic_index_in_dim(blocks, source, axis=0, keepdims=False)
        return jnp.einsum("chru,uk->hcrk", taken, weight, preferred_element_type=jnp.float32)

    partial = contribution(me_z, flat_own)
    for d in range(1, down):
        low, high = jnp.maximum(me_z - d, 0), jnp.minimum(me_z + d, down - 1)
        if 2 * d <= down - 1:
            partial = partial + contribution(low, below[d - 1])
            partial = partial + contribution(high, above[d - 1])
        else:
            use_low = me_z - d >= 0
            weight = jnp.where(use_low, below[d - 1], above[d - 1])
            partial = partial + contribution(jnp.where(use_low, low, high), weight)
    partial = partial.reshape(across, tok_rows, 3 * width_local)
    projected = lax.dynamic_index_in_dim(partial, me_x, axis=0, keepdims=False)
    for k in range(1, across):
        route = [(i, (i + k) % across) for i in range(across)]
        piece = lax.dynamic_index_in_dim(partial, (me_x + k) % across, axis=0, keepdims=False)
        projected = projected + lax.ppermute(piece, "x", route)
    streams = projected.astype(jnp.bfloat16).reshape(tok_rows, 3, width_local)
    tap_count = short_filter.shape[0]
    last_rows = streams[tok_rows - (tap_count - 1) :]
    before = from_behind(last_rows, SEQ, 1)
    padded = jnp.concatenate([before, streams], axis=0).astype(jnp.float32)
    filter_taps = short_filter.astype(jnp.float32)
    featured = jnp.zeros((tok_rows, 3, width_local), jnp.float32)
    for shift_back in range(tap_count):
        begin = tap_count - 1 - shift_back
        featured = featured + filter_taps[shift_back][None] * padded[begin : begin + tok_rows]
    query_gate = featured[:, 0]
    gated_rows = (featured[:, 1] * featured[:, 2]).astype(jnp.bfloat16)
    gated_wide = gated_rows.astype(jnp.float32)
    position = jnp.arange(tok_rows, dtype=jnp.float32)
    powers = jnp.exp(-decay_rate[None, :, :] * (tok_rows - 1.0 - position)[:, None, None])
    local_state = jnp.einsum("jc,jcr->cr", gated_wide, powers, precision=exact_mode)
    along = [local_state] + ring_sends(lambda k, p: local_state, "x", across)
    row = jnp.stack(along)
    states = jnp.stack([row] + ring_sends(lambda k, p: row, "zl", down))
    step_z = jnp.arange(down)[:, None]
    step_x = jnp.arange(across)[None, :]
    source = ((me_z - step_z) % down) * across + (me_x - step_x) % across
    lag = (me_z * across + me_x - 1 - source).astype(jnp.float32)
    decay_b = decay_rate[None, None]
    weight = jnp.exp(-decay_b * (float(tok_rows) * jnp.maximum(lag, 0.0))[:, :, None, None])
    weight = jnp.where((lag >= 0)[:, :, None, None], weight, 0.0)
    incoming = jnp.sum(weight * states, axis=(0, 1))
    growth = jnp.exp(decay_rate[None, :, :] * position[:, None, None])
    scaled = (gated_wide[:, :, None] * growth).reshape(tok_rows, width_local * mode_count)
    lower_mask = (jnp.arange(tok_rows)[:, None] >= jnp.arange(tok_rows)[None, :]).astype(
        jnp.float32
    )
    running_sum = jnp.dot(lower_mask, scaled, precision=exact_mode).reshape(
        tok_rows, width_local, mode_count
    )
    shrink = jnp.exp(-decay_rate[None, :, :] * position[:, None, None])
    entering = (incoming * jnp.exp(-decay_rate))[None]
    convolved = jnp.sum(residue[None] * shrink * (running_sum + entering), axis=2)
    long_mix = convolved + skip_gain[None, :] * gated_wide
    return (query_gate * long_mix).astype(jnp.bfloat16)


def split_mesh(mesh):
    ctx, ch = mesh.shape["ctx"], mesh.shape["ch"]
    devices = np.asarray(mesh.devices).reshape(ctx // 4, 4, ch // 4, 2, 2)
    return Mesh(devices, SEQ + CH)


def solution(mesh):
    fine = split_mesh(mesh)
    in_specs = (
        P(SEQ, CH),
        P(SEQ, None, CH),
        P(None, None, CH),
        P(CH, None),
        P(CH, None),
        P(CH),
    )
    out_specs = P(SEQ, CH)
    return jax.shard_map(block, mesh=fine, in_specs=in_specs, out_specs=out_specs, check_vma=False)
```

```python
import jax
import jax.numpy as jnp
import numpy as np
from jax import lax
from jax.sharding import Mesh, PartitionSpec as P

exact_mode = lax.Precision.HIGHEST
SEQ = ("zl", "x")
SUB = ("zh", "c")
CH = ("y", "zh", "c")


def from_behind(block, axis, distance):
    devices = range(lax.axis_size(axis))
    route = [(i - distance, i) for i in devices if i - distance in devices]
    return lax.ppermute(block, axis, route)


def ring_sends(pieces, axis, size):
    position = lax.axis_index(axis)
    received = []
    for k in range(1, size):
        route = [(i, (i + k) % size) for i in range(size)]
        received.append(lax.ppermute(pieces(k, position), axis, route))
    return received


def line_gather(piece, axis, size):
    below, above = [], []
    near_b = lax.ppermute(piece, axis, [(i, i + 1) for i in range(size - 1)])
    near_a = lax.ppermute(piece, axis, [(i + 1, i) for i in range(size - 1)])
    below.append(near_b)
    above.append(near_a)
    for d in range(2, size):
        near_b = lax.ppermute(near_b, axis, [(i, i + 1) for i in range(d - 1, size - 1)])
        near_a = lax.ppermute(near_a, axis, [(i + 1, i) for i in range(0, size - d)])
        below.append(near_b)
        above.append(near_a)
    return below, above


def block(tokens, in_weight, short_filter, decay_rate, residue, skip_gain):
    tok_rows = tokens.shape[0]
    width_local = in_weight.shape[2]
    mode_count = decay_rate.shape[1]
    feat_block = in_weight.shape[0]
    across, down = lax.axis_size("x"), lax.axis_size("zl")
    me_x, me_z = lax.axis_index("x"), lax.axis_index("zl")
    halves = lax.axis_size("zh")
    pair = lax.axis_size("c")
    me_h = lax.axis_index("zh")
    stream_count = in_weight.shape[1]
    order = tuple(range(1, stream_count)) + (0,)
    relays = {}
    for s in order:
        relays[s] = line_gather(in_weight[:, s, :], "zl", down)
    swap = [(a * across + b, b * across + a) for a in range(across) for b in range(across)]
    cross = [
        (a * across + b, b * across + ((a // pair + 1) % halves) * pair + a % pair)
        for a in range(across)
        for b in range(across)
    ]
    near = lax.ppermute(tokens, ("x",) + SUB, swap)
    far = lax.ppermute(tokens, ("x",) + SUB, cross)
    both = jnp.stack([jnp.where(me_h == 0, near, far), jnp.where(me_h == 0, far, near)])
    gathered = lax.all_gather(both, ("y", "c"), axis=0, tiled=False)
    blocks = gathered.reshape(-1, pair, halves, tok_rows, feat_block)

    def contribution(source, weight):
        taken = lax.dynamic_index_in_dim(blocks, source, axis=0, keepdims=False)
        return jnp.einsum("chru,uk->hcrk", taken, weight, preferred_element_type=jnp.float32)

    reduced = {}
    for s in order:
        below, above = relays[s]
        partial = contribution(me_z, in_weight[:, s, :])
        for d in range(1, down):
            low, high = jnp.maximum(me_z - d, 0), jnp.minimum(me_z + d, down - 1)
            if 2 * d <= down - 1:
                partial = partial + contribution(low, below[d - 1])
                partial = partial + contribution(high, above[d - 1])
            else:
                use_low = me_z - d >= 0
                weight = jnp.where(use_low, below[d - 1], above[d - 1])
                partial = partial + contribution(jnp.where(use_low, low, high), weight)
        partial = partial.reshape(across, tok_rows, width_local)
        total = lax.dynamic_index_in_dim(partial, me_x, axis=0, keepdims=False)
        for k in range(1, across):
            route = [(i, (i + k) % across) for i in range(across)]
            piece = lax.dynamic_index_in_dim(partial, (me_x + k) % across, axis=0, keepdims=False)
            total = total + lax.ppermute(piece, "x", route)
        reduced[s] = total
    projected = jnp.stack([reduced[s] for s in range(stream_count)], axis=1)
    streams = projected.astype(jnp.bfloat16)
    tap_count = short_filter.shape[0]
    last_rows = streams[tok_rows - (tap_count - 1) :]
    before = from_behind(last_rows, SEQ, 1)
    padded = jnp.concatenate([before, streams], axis=0).astype(jnp.float32)
    filter_taps = short_filter.astype(jnp.float32)
    featured = jnp.zeros((tok_rows, 3, width_local), jnp.float32)
    for shift_back in range(tap_count):
        begin = tap_count - 1 - shift_back
        featured = featured + filter_taps[shift_back][None] * padded[begin : begin + tok_rows]
    query_gate = featured[:, 0]
    gated_rows = (featured[:, 1] * featured[:, 2]).astype(jnp.bfloat16)
    gated_wide = gated_rows.astype(jnp.float32)
    position = jnp.arange(tok_rows, dtype=jnp.float32)
    powers = jnp.exp(-decay_rate[None, :, :] * (tok_rows - 1.0 - position)[:, None, None])
    local_state = jnp.einsum("jc,jcr->cr", gated_wide, powers, precision=exact_mode)
    along = [local_state] + ring_sends(lambda k, p: local_state, "x", across)
    row = jnp.stack(along)
    states = jnp.stack([row] + ring_sends(lambda k, p: row, "zl", down))
    step_z = jnp.arange(down)[:, None]
    step_x = jnp.arange(across)[None, :]
    source = ((me_z - step_z) % down) * across + (me_x - step_x) % across
    lag = (me_z * across + me_x - 1 - source).astype(jnp.float32)
    decay_b = decay_rate[None, None]
    weight = jnp.exp(-decay_b * (float(tok_rows) * jnp.maximum(lag, 0.0))[:, :, None, None])
    weight = jnp.where((lag >= 0)[:, :, None, None], weight, 0.0)
    incoming = jnp.sum(weight * states, axis=(0, 1))
    growth = jnp.exp(decay_rate[None, :, :] * position[:, None, None])
    scaled = (gated_wide[:, :, None] * growth).reshape(tok_rows, width_local * mode_count)
    lower_mask = (jnp.arange(tok_rows)[:, None] >= jnp.arange(tok_rows)[None, :]).astype(
        jnp.float32
    )
    running_sum = jnp.dot(lower_mask, scaled, precision=exact_mode).reshape(
        tok_rows, width_local, mode_count
    )
    shrink = jnp.exp(-decay_rate[None, :, :] * position[:, None, None])
    entering = (incoming * jnp.exp(-decay_rate))[None]
    convolved = jnp.sum(residue[None] * shrink * (running_sum + entering), axis=2)
    long_mix = convolved + skip_gain[None, :] * gated_wide
    return (query_gate * long_mix).astype(jnp.bfloat16)


def split_mesh(mesh):
    ctx, ch = mesh.shape["ctx"], mesh.shape["ch"]
    devices = np.asarray(mesh.devices).reshape(ctx // 4, 4, ch // 4, 2, 2)
    return Mesh(devices, SEQ + CH)


def solution(mesh):
    fine = split_mesh(mesh)
    in_specs = (
        P(SEQ, CH),
        P(SEQ, None, CH),
        P(None, None, CH),
        P(CH, None),
        P(CH, None),
        P(CH),
    )
    out_specs = P(SEQ, CH)
    return jax.shard_map(block, mesh=fine, in_specs=in_specs, out_specs=out_specs, check_vma=False)
```

```python
import jax
import jax.numpy as jnp
import numpy as np
from jax import lax
from jax.sharding import Mesh, PartitionSpec as P

exact_mode = lax.Precision.HIGHEST
SEQ = ("zl", "x")
SUB = ("zh", "c")
CH = ("y", "zh", "c")


def from_behind(block, axis, distance):
    devices = range(lax.axis_size(axis))
    route = [(i - distance, i) for i in devices if i - distance in devices]
    return lax.ppermute(block, axis, route)


def ring_sends(pieces, axis, size):
    position = lax.axis_index(axis)
    received = []
    for k in range(1, size):
        route = [(i, (i + k) % size) for i in range(size)]
        received.append(lax.ppermute(pieces(k, position), axis, route))
    return received


def line_gather(piece, axis, size):
    below, above = [], []
    near_b = lax.ppermute(piece, axis, [(i, i + 1) for i in range(size - 1)])
    near_a = lax.ppermute(piece, axis, [(i + 1, i) for i in range(size - 1)])
    below.append(near_b)
    above.append(near_a)
    for d in range(2, size):
        near_b = lax.ppermute(near_b, axis, [(i, i + 1) for i in range(d - 1, size - 1)])
        near_a = lax.ppermute(near_a, axis, [(i + 1, i) for i in range(0, size - d)])
        below.append(near_b)
        above.append(near_a)
    return below, above


def block(tokens, in_weight, short_filter, decay_rate, residue, skip_gain):
    tok_rows = tokens.shape[0]
    width_local = in_weight.shape[2]
    mode_count = decay_rate.shape[1]
    feat_block = in_weight.shape[0]
    across, down = lax.axis_size("x"), lax.axis_size("zl")
    me_x, me_z = lax.axis_index("x"), lax.axis_index("zl")
    halves = lax.axis_size("zh")
    pair = lax.axis_size("c")
    me_h = lax.axis_index("zh")
    stream_count = in_weight.shape[1]
    order = (tuple(range(1, stream_count)), (0,))
    relays = {}
    for s in order:
        own = in_weight[:, s[0] : s[-1] + 1, :].reshape(feat_block, len(s) * width_local)
        relays[s] = (own, line_gather(own, "zl", down))
    swap = [(a * across + b, b * across + a) for a in range(across) for b in range(across)]
    cross = [
        (a * across + b, b * across + ((a // pair + 1) % halves) * pair + a % pair)
        for a in range(across)
        for b in range(across)
    ]
    near = lax.ppermute(tokens, ("x",) + SUB, swap)
    far = lax.ppermute(tokens, ("x",) + SUB, cross)
    both = jnp.stack([jnp.where(me_h == 0, near, far), jnp.where(me_h == 0, far, near)])
    gathered = lax.all_gather(both, ("y", "c"), axis=0, tiled=False)
    blocks = gathered.reshape(-1, pair, halves, tok_rows, feat_block)

    def contribution(source, weight):
        taken = lax.dynamic_index_in_dim(blocks, source, axis=0, keepdims=False)
        return jnp.einsum("chru,uk->hcrk", taken, weight, preferred_element_type=jnp.float32)

    reduced = {}
    for s in order:
        own, (below, above) = relays[s]
        partial = contribution(me_z, own)
        for d in range(1, down):
            low, high = jnp.maximum(me_z - d, 0), jnp.minimum(me_z + d, down - 1)
            if 2 * d <= down - 1:
                partial = partial + contribution(low, below[d - 1])
                partial = partial + contribution(high, above[d - 1])
            else:
                use_low = me_z - d >= 0
                weight = jnp.where(use_low, below[d - 1], above[d - 1])
                partial = partial + contribution(jnp.where(use_low, low, high), weight)
        partial = partial.reshape(across, tok_rows, len(s) * width_local)
        total = lax.dynamic_index_in_dim(partial, me_x, axis=0, keepdims=False)
        for k in range(1, across):
            route = [(i, (i + k) % across) for i in range(across)]
            piece = lax.dynamic_index_in_dim(partial, (me_x + k) % across, axis=0, keepdims=False)
            total = total + lax.ppermute(piece, "x", route)
        for n, t in enumerate(s):
            reduced[t] = total[:, n * width_local : (n + 1) * width_local]
    projected = jnp.stack([reduced[t] for t in range(stream_count)], axis=1)
    streams = projected.astype(jnp.bfloat16)
    tap_count = short_filter.shape[0]
    last_rows = streams[tok_rows - (tap_count - 1) :]
    before = from_behind(last_rows, SEQ, 1)
    padded = jnp.concatenate([before, streams], axis=0).astype(jnp.float32)
    filter_taps = short_filter.astype(jnp.float32)
    featured = jnp.zeros((tok_rows, 3, width_local), jnp.float32)
    for shift_back in range(tap_count):
        begin = tap_count - 1 - shift_back
        featured = featured + filter_taps[shift_back][None] * padded[begin : begin + tok_rows]
    query_gate = featured[:, 0]
    gated_rows = (featured[:, 1] * featured[:, 2]).astype(jnp.bfloat16)
    gated_wide = gated_rows.astype(jnp.float32)
    position = jnp.arange(tok_rows, dtype=jnp.float32)
    powers = jnp.exp(-decay_rate[None, :, :] * (tok_rows - 1.0 - position)[:, None, None])
    local_state = jnp.einsum("jc,jcr->cr", gated_wide, powers, precision=exact_mode)
    along = [local_state] + ring_sends(lambda k, p: local_state, "x", across)
    row = jnp.stack(along)
    states = jnp.stack([row] + ring_sends(lambda k, p: row, "zl", down))
    step_z = jnp.arange(down)[:, None]
    step_x = jnp.arange(across)[None, :]
    source = ((me_z - step_z) % down) * across + (me_x - step_x) % across
    lag = (me_z * across + me_x - 1 - source).astype(jnp.float32)
    decay_b = decay_rate[None, None]
    weight = jnp.exp(-decay_b * (float(tok_rows) * jnp.maximum(lag, 0.0))[:, :, None, None])
    weight = jnp.where((lag >= 0)[:, :, None, None], weight, 0.0)
    incoming = jnp.sum(weight * states, axis=(0, 1))
    growth = jnp.exp(decay_rate[None, :, :] * position[:, None, None])
    scaled = (gated_wide[:, :, None] * growth).reshape(tok_rows, width_local * mode_count)
    lower_mask = (jnp.arange(tok_rows)[:, None] >= jnp.arange(tok_rows)[None, :]).astype(
        jnp.float32
    )
    running_sum = jnp.dot(lower_mask, scaled, precision=exact_mode).reshape(
        tok_rows, width_local, mode_count
    )
    shrink = jnp.exp(-decay_rate[None, :, :] * position[:, None, None])
    entering = (incoming * jnp.exp(-decay_rate))[None]
    convolved = jnp.sum(residue[None] * shrink * (running_sum + entering), axis=2)
    long_mix = convolved + skip_gain[None, :] * gated_wide
    return (query_gate * long_mix).astype(jnp.bfloat16)


def split_mesh(mesh):
    ctx, ch = mesh.shape["ctx"], mesh.shape["ch"]
    devices = np.asarray(mesh.devices).reshape(ctx // 4, 4, ch // 4, 2, 2)
    return Mesh(devices, SEQ + CH)


def solution(mesh):
    fine = split_mesh(mesh)
    in_specs = (
        P(SEQ, CH),
        P(SEQ, None, CH),
        P(None, None, CH),
        P(CH, None),
        P(CH, None),
        P(CH),
    )
    out_specs = P(SEQ, CH)
    return jax.shard_map(block, mesh=fine, in_specs=in_specs, out_specs=out_specs, check_vma=False)
```

```python
import jax
import jax.numpy as jnp
import numpy as np
from jax import lax
from jax.sharding import Mesh, PartitionSpec as P

exact_mode = lax.Precision.HIGHEST
SEQ = ("zl", "x")
SUB = ("zh", "c")
CH = ("y", "zh", "c")


def from_behind(block, axis, distance):
    devices = range(lax.axis_size(axis))
    route = [(i - distance, i) for i in devices if i - distance in devices]
    return lax.ppermute(block, axis, route)


def ring_sends(pieces, axis, size):
    position = lax.axis_index(axis)
    received = []
    for k in range(1, size):
        route = [(i, (i + k) % size) for i in range(size)]
        received.append(lax.ppermute(pieces(k, position), axis, route))
    return received


def line_gather(piece, axis, size):
    below, above = [], []
    near_b = lax.ppermute(piece, axis, [(i, i + 1) for i in range(size - 1)])
    near_a = lax.ppermute(piece, axis, [(i + 1, i) for i in range(size - 1)])
    below.append(near_b)
    above.append(near_a)
    for d in range(2, size):
        near_b = lax.ppermute(near_b, axis, [(i, i + 1) for i in range(d - 1, size - 1)])
        near_a = lax.ppermute(near_a, axis, [(i + 1, i) for i in range(0, size - d)])
        below.append(near_b)
        above.append(near_a)
    return below, above


def block(tokens, in_weight, short_filter, decay_rate, residue, skip_gain):
    tok_rows = tokens.shape[0]
    width_local = in_weight.shape[2]
    mode_count = decay_rate.shape[1]
    feat_block = in_weight.shape[0]
    across, down = lax.axis_size("x"), lax.axis_size("zl")
    me_x, me_z = lax.axis_index("x"), lax.axis_index("zl")
    halves = lax.axis_size("zh")
    pair = lax.axis_size("c")
    me_h = lax.axis_index("zh")
    stream_count = in_weight.shape[1]
    order = tuple(range(1, stream_count)) + (0,)
    relays = {}
    for s in order:
        relays[s] = line_gather(in_weight[:, s, :], "zl", down)
    swap = [(a * across + b, b * across + a) for a in range(across) for b in range(across)]
    cross = [
        (a * across + b, b * across + ((a // pair + 1) % halves) * pair + a % pair)
        for a in range(across)
        for b in range(across)
    ]
    near = lax.ppermute(tokens, ("x",) + SUB, swap)
    far = lax.ppermute(tokens, ("x",) + SUB, cross)
    both = jnp.stack([jnp.where(me_h == 0, near, far), jnp.where(me_h == 0, far, near)])
    gathered = lax.all_gather(both, ("y", "c"), axis=0, tiled=False)
    blocks = gathered.reshape(-1, pair, halves, tok_rows, feat_block)

    def contribution(source, weight):
        taken = lax.dynamic_index_in_dim(blocks, source, axis=0, keepdims=False)
        return jnp.einsum("chru,uk->hcrk", taken, weight, preferred_element_type=jnp.float32)

    reduced = {}
    for s in order:
        below, above = relays[s]
        partial = contribution(me_z, in_weight[:, s, :])
        for d in range(1, down):
            low, high = jnp.maximum(me_z - d, 0), jnp.minimum(me_z + d, down - 1)
            if 2 * d <= down - 1:
                partial = partial + contribution(low, below[d - 1])
                partial = partial + contribution(high, above[d - 1])
            else:
                use_low = me_z - d >= 0
                weight = jnp.where(use_low, below[d - 1], above[d - 1])
                partial = partial + contribution(jnp.where(use_low, low, high), weight)
        partial = partial.reshape(across, tok_rows, width_local)
        total = lax.dynamic_index_in_dim(partial, me_x, axis=0, keepdims=False)
        for k in range(1, across):
            route = [(i, (i + k) % across) for i in range(across)]
            piece = lax.dynamic_index_in_dim(partial, (me_x + k) % across, axis=0, keepdims=False)
            total = total + lax.ppermute(piece, "x", route)
        reduced[s] = total
    projected = jnp.stack([reduced[s] for s in range(stream_count)], axis=1)
    streams = projected.astype(jnp.bfloat16)
    tap_count = short_filter.shape[0]
    last_rows = streams[tok_rows - (tap_count - 1) :]
    before = from_behind(last_rows, SEQ, 1)
    padded = jnp.concatenate([before, streams], axis=0).astype(jnp.float32)
    filter_taps = short_filter.astype(jnp.float32)
    featured = jnp.zeros((tok_rows, 3, width_local), jnp.float32)
    for shift_back in range(tap_count):
        begin = tap_count - 1 - shift_back
        featured = featured + filter_taps[shift_back][None] * padded[begin : begin + tok_rows]
    query_gate = featured[:, 0]
    gated_rows = (featured[:, 1] * featured[:, 2]).astype(jnp.bfloat16)
    gated_wide = gated_rows.astype(jnp.float32)
    position = jnp.arange(tok_rows, dtype=jnp.float32)
    powers = jnp.exp(-decay_rate[None, :, :] * (tok_rows - 1.0 - position)[:, None, None])
    local_state = jnp.einsum("jc,jcr->cr", gated_wide, powers, precision=exact_mode)
    along = [local_state] + ring_sends(lambda k, p: local_state, "x", across)
    row = jnp.stack(along)
    states = jnp.stack([row] + ring_sends(lambda k, p: row, "zl", down))
    step_z = jnp.arange(down)[:, None]
    step_x = jnp.arange(across)[None, :]
    source = ((me_z - step_z) % down) * across + (me_x - step_x) % across
    lag = (me_z * across + me_x - 1 - source).astype(jnp.float32)
    decay_b = decay_rate[None, None]
    weight = jnp.exp(-decay_b * (float(tok_rows) * jnp.maximum(lag, 0.0))[:, :, None, None])
    weight = jnp.where((lag >= 0)[:, :, None, None], weight, 0.0)
    incoming = jnp.sum(weight * states, axis=(0, 1))
    growth = jnp.exp(decay_rate[None, :, :] * position[:, None, None])
    scaled = (gated_wide[:, :, None] * growth).reshape(tok_rows, width_local * mode_count)
    lower_mask = (jnp.arange(tok_rows)[:, None] >= jnp.arange(tok_rows)[None, :]).astype(
        jnp.float32
    )
    mask_b = lower_mask.astype(jnp.bfloat16)
    running_sum = jnp.zeros(scaled.shape, jnp.float32)
    rest = scaled
    for _ in range(3):
        part = rest.astype(jnp.bfloat16)
        running_sum = running_sum + jnp.dot(mask_b, part, preferred_element_type=jnp.float32)
        rest = rest - part.astype(jnp.float32)
    running_sum = running_sum.reshape(tok_rows, width_local, mode_count)
    shrink = jnp.exp(-decay_rate[None, :, :] * position[:, None, None])
    weighted = residue[None] * shrink
    inside = jnp.sum(weighted * running_sum, axis=2)
    entering = (incoming * jnp.exp(-decay_rate))[None]
    convolved = inside + jnp.sum(weighted * entering, axis=2)
    long_mix = convolved + skip_gain[None, :] * gated_wide
    return (query_gate * long_mix).astype(jnp.bfloat16)


def split_mesh(mesh):
    ctx, ch = mesh.shape["ctx"], mesh.shape["ch"]
    devices = np.asarray(mesh.devices).reshape(ctx // 4, 4, ch // 4, 2, 2)
    return Mesh(devices, SEQ + CH)


def solution(mesh):
    fine = split_mesh(mesh)
    in_specs = (
        P(SEQ, CH),
        P(SEQ, None, CH),
        P(None, None, CH),
        P(CH, None),
        P(CH, None),
        P(CH),
    )
    out_specs = P(SEQ, CH)
    return jax.shard_map(block, mesh=fine, in_specs=in_specs, out_specs=out_specs, check_vma=False)
```

```python
import jax
import jax.numpy as jnp
import numpy as np
from jax import lax
from jax.sharding import Mesh, PartitionSpec as P

exact_mode = lax.Precision.HIGHEST
SEQ = ("zl", "x")
SUB = ("zh", "c")
CH = ("y", "zh", "c")


def from_behind(block, axis, distance):
    devices = range(lax.axis_size(axis))
    route = [(i - distance, i) for i in devices if i - distance in devices]
    return lax.ppermute(block, axis, route)


def ring_sends(pieces, axis, size):
    position = lax.axis_index(axis)
    received = []
    for k in range(1, size):
        route = [(i, (i + k) % size) for i in range(size)]
        received.append(lax.ppermute(pieces(k, position), axis, route))
    return received


def line_gather(piece, axis, size):
    below, above = [], []
    near_b = lax.ppermute(piece, axis, [(i, i + 1) for i in range(size - 1)])
    near_a = lax.ppermute(piece, axis, [(i + 1, i) for i in range(size - 1)])
    below.append(near_b)
    above.append(near_a)
    for d in range(2, size):
        near_b = lax.ppermute(near_b, axis, [(i, i + 1) for i in range(d - 1, size - 1)])
        near_a = lax.ppermute(near_a, axis, [(i + 1, i) for i in range(0, size - d)])
        below.append(near_b)
        above.append(near_a)
    return below, above


def block(tokens, in_weight, short_filter, decay_rate, residue, skip_gain):
    tok_rows = tokens.shape[0]
    width_local = in_weight.shape[2]
    mode_count = decay_rate.shape[1]
    feat_block = in_weight.shape[0]
    across, down = lax.axis_size("x"), lax.axis_size("zl")
    me_x, me_z = lax.axis_index("x"), lax.axis_index("zl")
    halves = lax.axis_size("zh")
    pair = lax.axis_size("c")
    me_h = lax.axis_index("zh")
    stream_count = in_weight.shape[1]
    order = tuple(range(1, stream_count)) + (0,)
    relays = {}
    for s in order:
        relays[s] = line_gather(in_weight[:, s, :], "zl", down)
    swap = [(a * across + b, b * across + a) for a in range(across) for b in range(across)]
    cross = [
        (a * across + b, b * across + ((a // pair + 1) % halves) * pair + a % pair)
        for a in range(across)
        for b in range(across)
    ]
    near = lax.ppermute(tokens, ("x",) + SUB, swap)
    far = lax.ppermute(tokens, ("x",) + SUB, cross)
    both = jnp.stack([jnp.where(me_h == 0, near, far), jnp.where(me_h == 0, far, near)])
    gathered = lax.all_gather(both, ("y", "c"), axis=0, tiled=False)
    blocks = gathered.reshape(-1, pair, halves, tok_rows, feat_block)

    def contribution(source, weight):
        taken = lax.dynamic_index_in_dim(blocks, source, axis=0, keepdims=False)
        return jnp.einsum("chru,uk->hcrk", taken, weight, preferred_element_type=jnp.float32)

    reduced = {}
    for s in order:
        below, above = relays[s]
        partial = contribution(me_z, in_weight[:, s, :])
        for d in range(1, down):
            low, high = jnp.maximum(me_z - d, 0), jnp.minimum(me_z + d, down - 1)
            if 2 * d <= down - 1:
                partial = partial + contribution(low, below[d - 1])
                partial = partial + contribution(high, above[d - 1])
            else:
                use_low = me_z - d >= 0
                weight = jnp.where(use_low, below[d - 1], above[d - 1])
                partial = partial + contribution(jnp.where(use_low, low, high), weight)
        partial = partial.reshape(across, tok_rows, width_local)
        total = lax.dynamic_index_in_dim(partial, me_x, axis=0, keepdims=False)
        for k in range(1, across):
            route = [(i, (i + k) % across) for i in range(across)]
            piece = lax.dynamic_index_in_dim(partial, (me_x + k) % across, axis=0, keepdims=False)
            total = total + lax.ppermute(piece, "x", route)
        reduced[s] = total
    tap_count = short_filter.shape[0]
    filter_taps = short_filter.astype(jnp.float32)

    def short_conv(group):
        streams = jnp.stack([reduced[t] for t in group], axis=1).astype(jnp.bfloat16)
        last_rows = streams[tok_rows - (tap_count - 1) :]
        before = from_behind(last_rows, SEQ, 1)
        padded = jnp.concatenate([before, streams], axis=0).astype(jnp.float32)
        taps = filter_taps[:, group[0] : group[-1] + 1]
        featured = jnp.zeros((tok_rows, len(group), width_local), jnp.float32)
        for shift_back in range(tap_count):
            begin = tap_count - 1 - shift_back
            featured = featured + taps[shift_back][None] * padded[begin : begin + tok_rows]
        return featured

    gates = short_conv(order[:-1])
    gated_rows = (gates[:, 0] * gates[:, 1]).astype(jnp.bfloat16)
    gated_wide = gated_rows.astype(jnp.float32)
    position = jnp.arange(tok_rows, dtype=jnp.float32)
    powers = jnp.exp(-decay_rate[None, :, :] * (tok_rows - 1.0 - position)[:, None, None])
    local_state = jnp.einsum("jc,jcr->cr", gated_wide, powers, precision=exact_mode)
    along = [local_state] + ring_sends(lambda k, p: local_state, "x", across)
    row = jnp.stack(along)
    states = jnp.stack([row] + ring_sends(lambda k, p: row, "zl", down))
    step_z = jnp.arange(down)[:, None]
    step_x = jnp.arange(across)[None, :]
    source = ((me_z - step_z) % down) * across + (me_x - step_x) % across
    lag = (me_z * across + me_x - 1 - source).astype(jnp.float32)
    decay_b = decay_rate[None, None]
    weight = jnp.exp(-decay_b * (float(tok_rows) * jnp.maximum(lag, 0.0))[:, :, None, None])
    weight = jnp.where((lag >= 0)[:, :, None, None], weight, 0.0)
    incoming = jnp.sum(weight * states, axis=(0, 1))
    growth = jnp.exp(decay_rate[None, :, :] * position[:, None, None])
    scaled = (gated_wide[:, :, None] * growth).reshape(tok_rows, width_local * mode_count)
    lower_mask = (jnp.arange(tok_rows)[:, None] >= jnp.arange(tok_rows)[None, :]).astype(
        jnp.float32
    )
    running_sum = jnp.dot(lower_mask, scaled, precision=exact_mode).reshape(
        tok_rows, width_local, mode_count
    )
    shrink = jnp.exp(-decay_rate[None, :, :] * position[:, None, None])
    weighted = residue[None] * shrink
    inside = jnp.sum(weighted * running_sum, axis=2)
    entering = (incoming * jnp.exp(-decay_rate))[None]
    convolved = inside + jnp.sum(weighted * entering, axis=2)
    long_mix = convolved + skip_gain[None, :] * gated_wide
    query_gate = short_conv(order[-1:])[:, 0]
    return (query_gate * long_mix).astype(jnp.bfloat16)


def split_mesh(mesh):
    ctx, ch = mesh.shape["ctx"], mesh.shape["ch"]
    devices = np.asarray(mesh.devices).reshape(ctx // 4, 4, ch // 4, 2, 2)
    return Mesh(devices, SEQ + CH)


def solution(mesh):
    fine = split_mesh(mesh)
    in_specs = (
        P(SEQ, CH),
        P(SEQ, None, CH),
        P(None, None, CH),
        P(CH, None),
        P(CH, None),
        P(CH),
    )
    out_specs = P(SEQ, CH)
    return jax.shard_map(block, mesh=fine, in_specs=in_specs, out_specs=out_specs, check_vma=False)
```

```python
import jax
import jax.numpy as jnp
import numpy as np
from jax import lax
from jax.sharding import Mesh, PartitionSpec as P

exact_mode = lax.Precision.HIGHEST
SEQ = ("zl", "x")
SUB = ("zh", "c")
CH = ("y", "zh", "c")


def from_behind(block, axis, distance):
    devices = range(lax.axis_size(axis))
    route = [(i - distance, i) for i in devices if i - distance in devices]
    return lax.ppermute(block, axis, route)


def ring_sends(pieces, axis, size):
    position = lax.axis_index(axis)
    received = []
    for k in range(1, size):
        route = [(i, (i + k) % size) for i in range(size)]
        received.append(lax.ppermute(pieces(k, position), axis, route))
    return received


def line_gather(piece, axis, size):
    below, above = [], []
    near_b = lax.ppermute(piece, axis, [(i, i + 1) for i in range(size - 1)])
    near_a = lax.ppermute(piece, axis, [(i + 1, i) for i in range(size - 1)])
    below.append(near_b)
    above.append(near_a)
    for d in range(2, size):
        near_b = lax.ppermute(near_b, axis, [(i, i + 1) for i in range(d - 1, size - 1)])
        near_a = lax.ppermute(near_a, axis, [(i + 1, i) for i in range(0, size - d)])
        below.append(near_b)
        above.append(near_a)
    return below, above


def block(tokens, in_weight, short_filter, decay_rate, residue, skip_gain):
    tok_rows = tokens.shape[0]
    width_local = in_weight.shape[2]
    mode_count = decay_rate.shape[1]
    feat_block = in_weight.shape[0]
    across, down = lax.axis_size("x"), lax.axis_size("zl")
    me_x, me_z = lax.axis_index("x"), lax.axis_index("zl")
    halves = lax.axis_size("zh")
    pair = lax.axis_size("c")
    me_h = lax.axis_index("zh")
    stream_count = in_weight.shape[1]
    order = (tuple(range(1, stream_count)), (0,))
    relays = {}
    for s in order:
        own = in_weight[:, s[0] : s[-1] + 1, :].reshape(feat_block, len(s) * width_local)
        relays[s] = (own, line_gather(own, "zl", down))
    swap = [(a * across + b, b * across + a) for a in range(across) for b in range(across)]
    cross = [
        (a * across + b, b * across + ((a // pair + 1) % halves) * pair + a % pair)
        for a in range(across)
        for b in range(across)
    ]
    near = lax.ppermute(tokens, ("x",) + SUB, swap)
    far = lax.ppermute(tokens, ("x",) + SUB, cross)
    both = jnp.stack([jnp.where(me_h == 0, near, far), jnp.where(me_h == 0, far, near)])
    gathered = lax.all_gather(both, ("y", "c"), axis=0, tiled=False)
    blocks = gathered.reshape(-1, pair, halves, tok_rows, feat_block)

    def contribution(source, weight):
        taken = lax.dynamic_index_in_dim(blocks, source, axis=0, keepdims=False)
        return jnp.einsum("chru,uk->hcrk", taken, weight, preferred_element_type=jnp.float32)

    reduced = {}
    for s in order:
        own, (below, above) = relays[s]
        partial = contribution(me_z, own)
        for d in range(1, down):
            low, high = jnp.maximum(me_z - d, 0), jnp.minimum(me_z + d, down - 1)
            if 2 * d <= down - 1:
                partial = partial + contribution(low, below[d - 1])
                partial = partial + contribution(high, above[d - 1])
            else:
                use_low = me_z - d >= 0
                weight = jnp.where(use_low, below[d - 1], above[d - 1])
                partial = partial + contribution(jnp.where(use_low, low, high), weight)
        partial = partial.reshape(across, tok_rows, len(s) * width_local)
        total = lax.dynamic_index_in_dim(partial, me_x, axis=0, keepdims=False)
        for k in range(1, across):
            route = [(i, (i + k) % across) for i in range(across)]
            piece = lax.dynamic_index_in_dim(partial, (me_x + k) % across, axis=0, keepdims=False)
            total = total + lax.ppermute(piece, "x", route)
        for n, t in enumerate(s):
            reduced[t] = total[:, n * width_local : (n + 1) * width_local]
    tap_count = short_filter.shape[0]
    filter_taps = short_filter.astype(jnp.float32)

    def short_conv(group):
        streams = jnp.stack([reduced[t] for t in group], axis=1).astype(jnp.bfloat16)
        last_rows = streams[tok_rows - (tap_count - 1) :]
        before = from_behind(last_rows, SEQ, 1)
        padded = jnp.concatenate([before, streams], axis=0).astype(jnp.float32)
        taps = filter_taps[:, group[0] : group[-1] + 1]
        featured = jnp.zeros((tok_rows, len(group), width_local), jnp.float32)
        for shift_back in range(tap_count):
            begin = tap_count - 1 - shift_back
            featured = featured + taps[shift_back][None] * padded[begin : begin + tok_rows]
        return featured

    gates = short_conv(order[0])
    gated_rows = (gates[:, 0] * gates[:, 1]).astype(jnp.bfloat16)
    gated_wide = gated_rows.astype(jnp.float32)
    position = jnp.arange(tok_rows, dtype=jnp.float32)
    powers = jnp.exp(-decay_rate[None, :, :] * (tok_rows - 1.0 - position)[:, None, None])
    local_state = jnp.einsum("jc,jcr->cr", gated_wide, powers, precision=exact_mode)
    along = [local_state] + ring_sends(lambda k, p: local_state, "x", across)
    row = jnp.stack(along)
    states = jnp.stack([row] + ring_sends(lambda k, p: row, "zl", down))
    step_z = jnp.arange(down)[:, None]
    step_x = jnp.arange(across)[None, :]
    source = ((me_z - step_z) % down) * across + (me_x - step_x) % across
    lag = (me_z * across + me_x - 1 - source).astype(jnp.float32)
    decay_b = decay_rate[None, None]
    weight = jnp.exp(-decay_b * (float(tok_rows) * jnp.maximum(lag, 0.0))[:, :, None, None])
    weight = jnp.where((lag >= 0)[:, :, None, None], weight, 0.0)
    incoming = jnp.sum(weight * states, axis=(0, 1))
    growth = jnp.exp(decay_rate[None, :, :] * position[:, None, None])
    scaled = (gated_wide[:, :, None] * growth).reshape(tok_rows, width_local * mode_count)
    lower_mask = (jnp.arange(tok_rows)[:, None] >= jnp.arange(tok_rows)[None, :]).astype(
        jnp.float32
    )
    running_sum = jnp.dot(lower_mask, scaled, precision=exact_mode).reshape(
        tok_rows, width_local, mode_count
    )
    shrink = jnp.exp(-decay_rate[None, :, :] * position[:, None, None])
    entering = (incoming * jnp.exp(-decay_rate))[None]
    convolved = jnp.sum(residue[None] * shrink * (running_sum + entering), axis=2)
    long_mix = convolved + skip_gain[None, :] * gated_wide
    query_gate = short_conv(order[1])[:, 0]
    return (query_gate * long_mix).astype(jnp.bfloat16)


def split_mesh(mesh):
    ctx, ch = mesh.shape["ctx"], mesh.shape["ch"]
    devices = np.asarray(mesh.devices).reshape(ctx // 4, 4, ch // 4, 2, 2)
    return Mesh(devices, SEQ + CH)


def solution(mesh):
    fine = split_mesh(mesh)
    in_specs = (
        P(SEQ, CH),
        P(SEQ, None, CH),
        P(None, None, CH),
        P(CH, None),
        P(CH, None),
        P(CH),
    )
    out_specs = P(SEQ, CH)
    return jax.shard_map(block, mesh=fine, in_specs=in_specs, out_specs=out_specs, check_vma=False)
```

```python
import jax
import jax.numpy as jnp
import numpy as np
from jax import lax
from jax.sharding import Mesh, PartitionSpec as P

exact_mode = lax.Precision.HIGHEST
SEQ = ("zl", "x")
SUB = ("zh", "c")
CH = ("y", "zh", "c")


def from_behind(block, axis, distance):
    devices = range(lax.axis_size(axis))
    route = [(i - distance, i) for i in devices if i - distance in devices]
    return lax.ppermute(block, axis, route)


def ring_sends(pieces, axis, size):
    position = lax.axis_index(axis)
    received = []
    for k in range(1, size):
        route = [(i, (i + k) % size) for i in range(size)]
        received.append(lax.ppermute(pieces(k, position), axis, route))
    return received


def line_gather(piece, axis, size):
    below, above = [], []
    near_b = lax.ppermute(piece, axis, [(i, i + 1) for i in range(size - 1)])
    near_a = lax.ppermute(piece, axis, [(i + 1, i) for i in range(size - 1)])
    below.append(near_b)
    above.append(near_a)
    for d in range(2, size):
        near_b = lax.ppermute(near_b, axis, [(i, i + 1) for i in range(d - 1, size - 1)])
        near_a = lax.ppermute(near_a, axis, [(i + 1, i) for i in range(0, size - d)])
        below.append(near_b)
        above.append(near_a)
    return below, above


def block(tokens, in_weight, short_filter, decay_rate, residue, skip_gain):
    tok_rows = tokens.shape[0]
    width_local = in_weight.shape[2]
    mode_count = decay_rate.shape[1]
    feat_block = in_weight.shape[0]
    across, down = lax.axis_size("x"), lax.axis_size("zl")
    me_x, me_z = lax.axis_index("x"), lax.axis_index("zl")
    halves = lax.axis_size("zh")
    pair = lax.axis_size("c")
    me_h = lax.axis_index("zh")
    stream_count = in_weight.shape[1]
    order = tuple(range(1, stream_count)) + (0,)
    pieces = 2
    span = width_local // pieces
    relays = {}
    for s in order:
        for h in range(pieces):
            own = in_weight[:, s, h * span : (h + 1) * span]
            relays[s, h] = (own, line_gather(own, "zl", down))
    swap = [(a * across + b, b * across + a) for a in range(across) for b in range(across)]
    cross = [
        (a * across + b, b * across + ((a // pair + 1) % halves) * pair + a % pair)
        for a in range(across)
        for b in range(across)
    ]
    near = lax.ppermute(tokens, ("x",) + SUB, swap)
    far = lax.ppermute(tokens, ("x",) + SUB, cross)
    both = jnp.stack([jnp.where(me_h == 0, near, far), jnp.where(me_h == 0, far, near)])
    gathered = lax.all_gather(both, ("y", "c"), axis=0, tiled=False)
    blocks = gathered.reshape(-1, pair, halves, tok_rows, feat_block)

    def contribution(source, weight):
        taken = lax.dynamic_index_in_dim(blocks, source, axis=0, keepdims=False)
        return jnp.einsum("chru,uk->hcrk", taken, weight, preferred_element_type=jnp.float32)

    reduced = {}
    for s in order:
        halves_out = []
        for h in range(pieces):
            own, (below, above) = relays[s, h]
            partial = contribution(me_z, own)
            for d in range(1, down):
                low, high = jnp.maximum(me_z - d, 0), jnp.minimum(me_z + d, down - 1)
                if 2 * d <= down - 1:
                    partial = partial + contribution(low, below[d - 1])
                    partial = partial + contribution(high, above[d - 1])
                else:
                    use_low = me_z - d >= 0
                    weight = jnp.where(use_low, below[d - 1], above[d - 1])
                    partial = partial + contribution(jnp.where(use_low, low, high), weight)
            halves_out.append(partial)
        partial = jnp.concatenate(halves_out, axis=-1)
        partial = partial.reshape(across, tok_rows, width_local)
        total = lax.dynamic_index_in_dim(partial, me_x, axis=0, keepdims=False)
        for k in range(1, across):
            route = [(i, (i + k) % across) for i in range(across)]
            piece = lax.dynamic_index_in_dim(partial, (me_x + k) % across, axis=0, keepdims=False)
            total = total + lax.ppermute(piece, "x", route)
        reduced[s] = total
    tap_count = short_filter.shape[0]
    filter_taps = short_filter.astype(jnp.float32)

    def short_conv(group):
        streams = jnp.stack([reduced[t] for t in group], axis=1).astype(jnp.bfloat16)
        last_rows = streams[tok_rows - (tap_count - 1) :]
        before = from_behind(last_rows, SEQ, 1)
        padded = jnp.concatenate([before, streams], axis=0).astype(jnp.float32)
        taps = filter_taps[:, group[0] : group[-1] + 1]
        featured = jnp.zeros((tok_rows, len(group), width_local), jnp.float32)
        for shift_back in range(tap_count):
            begin = tap_count - 1 - shift_back
            featured = featured + taps[shift_back][None] * padded[begin : begin + tok_rows]
        return featured

    gates = short_conv(order[:-1])
    gated_rows = (gates[:, 0] * gates[:, 1]).astype(jnp.bfloat16)
    gated_wide = gated_rows.astype(jnp.float32)
    position = jnp.arange(tok_rows, dtype=jnp.float32)
    powers = jnp.exp(-decay_rate[None, :, :] * (tok_rows - 1.0 - position)[:, None, None])
    local_state = jnp.einsum("jc,jcr->cr", gated_wide, powers, precision=exact_mode)
    along = [local_state] + ring_sends(lambda k, p: local_state, "x", across)
    row = jnp.stack(along)
    states = jnp.stack([row] + ring_sends(lambda k, p: row, "zl", down))
    step_z = jnp.arange(down)[:, None]
    step_x = jnp.arange(across)[None, :]
    source = ((me_z - step_z) % down) * across + (me_x - step_x) % across
    lag = (me_z * across + me_x - 1 - source).astype(jnp.float32)
    decay_b = decay_rate[None, None]
    weight = jnp.exp(-decay_b * (float(tok_rows) * jnp.maximum(lag, 0.0))[:, :, None, None])
    weight = jnp.where((lag >= 0)[:, :, None, None], weight, 0.0)
    incoming = jnp.sum(weight * states, axis=(0, 1))
    growth = jnp.exp(decay_rate[None, :, :] * position[:, None, None])
    scaled = (gated_wide[:, :, None] * growth).reshape(tok_rows, width_local * mode_count)
    lower_mask = (jnp.arange(tok_rows)[:, None] >= jnp.arange(tok_rows)[None, :]).astype(
        jnp.float32
    )
    running_sum = jnp.dot(lower_mask, scaled, precision=exact_mode).reshape(
        tok_rows, width_local, mode_count
    )
    shrink = jnp.exp(-decay_rate[None, :, :] * position[:, None, None])
    entering = (incoming * jnp.exp(-decay_rate))[None]
    convolved = jnp.sum(residue[None] * shrink * (running_sum + entering), axis=2)
    long_mix = convolved + skip_gain[None, :] * gated_wide
    query_gate = short_conv(order[-1:])[:, 0]
    return (query_gate * long_mix).astype(jnp.bfloat16)


def split_mesh(mesh):
    ctx, ch = mesh.shape["ctx"], mesh.shape["ch"]
    devices = np.asarray(mesh.devices).reshape(ctx // 4, 4, ch // 4, 2, 2)
    return Mesh(devices, SEQ + CH)


def solution(mesh):
    fine = split_mesh(mesh)
    in_specs = (
        P(SEQ, CH),
        P(SEQ, None, CH),
        P(None, None, CH),
        P(CH, None),
        P(CH, None),
        P(CH),
    )
    out_specs = P(SEQ, CH)
    return jax.shard_map(block, mesh=fine, in_specs=in_specs, out_specs=out_specs, check_vma=False)
```

```python
import jax
import jax.numpy as jnp
import numpy as np
from jax import lax
from jax.sharding import Mesh, PartitionSpec as P

exact_mode = lax.Precision.HIGHEST
SEQ = ("zl", "x")
SUB = ("zh", "c")
CH = ("y", "zh", "c")


def from_behind(block, axis, distance):
    devices = range(lax.axis_size(axis))
    route = [(i - distance, i) for i in devices if i - distance in devices]
    return lax.ppermute(block, axis, route)


def ring_sends(pieces, axis, size):
    position = lax.axis_index(axis)
    received = []
    for k in range(1, size):
        route = [(i, (i + k) % size) for i in range(size)]
        received.append(lax.ppermute(pieces(k, position), axis, route))
    return received


def line_gather(piece, axis, size):
    below, above = [], []
    near_b = lax.ppermute(piece, axis, [(i, i + 1) for i in range(size - 1)])
    near_a = lax.ppermute(piece, axis, [(i + 1, i) for i in range(size - 1)])
    below.append(near_b)
    above.append(near_a)
    for d in range(2, size):
        near_b = lax.ppermute(near_b, axis, [(i, i + 1) for i in range(d - 1, size - 1)])
        near_a = lax.ppermute(near_a, axis, [(i + 1, i) for i in range(0, size - d)])
        below.append(near_b)
        above.append(near_a)
    return below, above


def block(tokens, in_weight, short_filter, decay_rate, residue, skip_gain):
    tok_rows = tokens.shape[0]
    width_local = in_weight.shape[2]
    mode_count = decay_rate.shape[1]
    feat_block = in_weight.shape[0]
    across, down = lax.axis_size("x"), lax.axis_size("zl")
    me_x, me_z = lax.axis_index("x"), lax.axis_index("zl")
    halves = lax.axis_size("zh")
    pair = lax.axis_size("c")
    me_h = lax.axis_index("zh")
    stream_count = in_weight.shape[1]
    order = tuple(range(1, stream_count)) + (0,)
    relays = {}
    for s in order:
        relays[s] = line_gather(in_weight[:, s, :], "zl", down)
    swap = [(a * across + b, b * across + a) for a in range(across) for b in range(across)]
    cross = [
        (a * across + b, b * across + ((a // pair + 1) % halves) * pair + a % pair)
        for a in range(across)
        for b in range(across)
    ]
    near = lax.ppermute(tokens, ("x",) + SUB, swap)
    far = lax.ppermute(tokens, ("x",) + SUB, cross)
    near_all = lax.all_gather(near, ("y", "c"), axis=0, tiled=False)
    far_all = lax.all_gather(far, ("y", "c"), axis=0, tiled=False)
    near_blocks = near_all.reshape(-1, pair, tok_rows, feat_block)
    far_blocks = far_all.reshape(-1, pair, tok_rows, feat_block)

    def contribution(source, weight):
        parts = []
        for copy in (near_blocks, far_blocks):
            taken = lax.dynamic_index_in_dim(copy, source, axis=0, keepdims=False)
            parts.append(
                jnp.einsum("cru,uk->crk", taken, weight, preferred_element_type=jnp.float32)
            )
        own_half, other_half = parts
        low_half = jnp.where(me_h == 0, own_half, other_half)
        high_half = jnp.where(me_h == 0, other_half, own_half)
        return jnp.stack([low_half, high_half])

    reduced = {}
    for s in order:
        below, above = relays[s]
        partial = contribution(me_z, in_weight[:, s, :])
        for d in range(1, down):
            low, high = jnp.maximum(me_z - d, 0), jnp.minimum(me_z + d, down - 1)
            if 2 * d <= down - 1:
                partial = partial + contribution(low, below[d - 1])
                partial = partial + contribution(high, above[d - 1])
            else:
                use_low = me_z - d >= 0
                weight = jnp.where(use_low, below[d - 1], above[d - 1])
                partial = partial + contribution(jnp.where(use_low, low, high), weight)
        partial = partial.reshape(across, tok_rows, width_local)
        total = lax.dynamic_index_in_dim(partial, me_x, axis=0, keepdims=False)
        for k in range(1, across):
            route = [(i, (i + k) % across) for i in range(across)]
            piece = lax.dynamic_index_in_dim(partial, (me_x + k) % across, axis=0, keepdims=False)
            total = total + lax.ppermute(piece, "x", route)
        reduced[s] = total
    tap_count = short_filter.shape[0]
    filter_taps = short_filter.astype(jnp.float32)

    def short_conv(group):
        streams = jnp.stack([reduced[t] for t in group], axis=1).astype(jnp.bfloat16)
        last_rows = streams[tok_rows - (tap_count - 1) :]
        before = from_behind(last_rows, SEQ, 1)
        padded = jnp.concatenate([before, streams], axis=0).astype(jnp.float32)
        taps = filter_taps[:, group[0] : group[-1] + 1]
        featured = jnp.zeros((tok_rows, len(group), width_local), jnp.float32)
        for shift_back in range(tap_count):
            begin = tap_count - 1 - shift_back
            featured = featured + taps[shift_back][None] * padded[begin : begin + tok_rows]
        return featured

    gates = short_conv(order[:-1])
    gated_rows = (gates[:, 0] * gates[:, 1]).astype(jnp.bfloat16)
    gated_wide = gated_rows.astype(jnp.float32)
    position = jnp.arange(tok_rows, dtype=jnp.float32)
    powers = jnp.exp(-decay_rate[None, :, :] * (tok_rows - 1.0 - position)[:, None, None])
    local_state = jnp.einsum("jc,jcr->cr", gated_wide, powers, precision=exact_mode)
    along = [local_state] + ring_sends(lambda k, p: local_state, "x", across)
    row = jnp.stack(along)
    states = jnp.stack([row] + ring_sends(lambda k, p: row, "zl", down))
    step_z = jnp.arange(down)[:, None]
    step_x = jnp.arange(across)[None, :]
    source = ((me_z - step_z) % down) * across + (me_x - step_x) % across
    lag = (me_z * across + me_x - 1 - source).astype(jnp.float32)
    decay_b = decay_rate[None, None]
    weight = jnp.exp(-decay_b * (float(tok_rows) * jnp.maximum(lag, 0.0))[:, :, None, None])
    weight = jnp.where((lag >= 0)[:, :, None, None], weight, 0.0)
    incoming = jnp.sum(weight * states, axis=(0, 1))
    growth = jnp.exp(decay_rate[None, :, :] * position[:, None, None])
    scaled = (gated_wide[:, :, None] * growth).reshape(tok_rows, width_local * mode_count)
    lower_mask = (jnp.arange(tok_rows)[:, None] >= jnp.arange(tok_rows)[None, :]).astype(
        jnp.float32
    )
    running_sum = jnp.dot(lower_mask, scaled, precision=exact_mode).reshape(
        tok_rows, width_local, mode_count
    )
    shrink = jnp.exp(-decay_rate[None, :, :] * position[:, None, None])
    entering = (incoming * jnp.exp(-decay_rate))[None]
    convolved = jnp.sum(residue[None] * shrink * (running_sum + entering), axis=2)
    long_mix = convolved + skip_gain[None, :] * gated_wide
    query_gate = short_conv(order[-1:])[:, 0]
    return (query_gate * long_mix).astype(jnp.bfloat16)


def split_mesh(mesh):
    ctx, ch = mesh.shape["ctx"], mesh.shape["ch"]
    devices = np.asarray(mesh.devices).reshape(ctx // 4, 4, ch // 4, 2, 2)
    return Mesh(devices, SEQ + CH)


def solution(mesh):
    fine = split_mesh(mesh)
    in_specs = (
        P(SEQ, CH),
        P(SEQ, None, CH),
        P(None, None, CH),
        P(CH, None),
        P(CH, None),
        P(CH),
    )
    out_specs = P(SEQ, CH)
    return jax.shard_map(block, mesh=fine, in_specs=in_specs, out_specs=out_specs, check_vma=False)
```

```python
import jax
import jax.numpy as jnp
import numpy as np
from jax import lax
from jax.sharding import Mesh, PartitionSpec as P

exact_mode = lax.Precision.HIGHEST
SEQ = ("zl", "x")
SUB = ("zh", "c")
CH = ("y", "zh", "c")


def from_behind(block, axis, distance):
    devices = range(lax.axis_size(axis))
    route = [(i - distance, i) for i in devices if i - distance in devices]
    return lax.ppermute(block, axis, route)


def ring_sends(pieces, axis, size):
    position = lax.axis_index(axis)
    received = []
    for k in range(1, size):
        route = [(i, (i + k) % size) for i in range(size)]
        received.append(lax.ppermute(pieces(k, position), axis, route))
    return received


def line_gather(piece, axis, size):
    below, above = [], []
    near_b = lax.ppermute(piece, axis, [(i, i + 1) for i in range(size - 1)])
    near_a = lax.ppermute(piece, axis, [(i + 1, i) for i in range(size - 1)])
    below.append(near_b)
    above.append(near_a)
    for d in range(2, size):
        near_b = lax.ppermute(near_b, axis, [(i, i + 1) for i in range(d - 1, size - 1)])
        near_a = lax.ppermute(near_a, axis, [(i + 1, i) for i in range(0, size - d)])
        below.append(near_b)
        above.append(near_a)
    return below, above


def block(tokens, in_weight, short_filter, decay_rate, residue, skip_gain):
    tok_rows = tokens.shape[0]
    width_local = in_weight.shape[2]
    mode_count = decay_rate.shape[1]
    feat_block = in_weight.shape[0]
    across, down = lax.axis_size("x"), lax.axis_size("zl")
    me_x, me_z = lax.axis_index("x"), lax.axis_index("zl")
    halves = lax.axis_size("zh")
    pair = lax.axis_size("c")
    me_h = lax.axis_index("zh")
    stream_count = in_weight.shape[1]
    order = tuple(range(1, stream_count)) + (0,)
    relays = {}
    for s in order:
        relays[s] = line_gather(in_weight[:, s, :], "zl", down)
    swap = [(a * across + b, b * across + a) for a in range(across) for b in range(across)]
    cross = [
        (a * across + b, b * across + ((a // pair + 1) % halves) * pair + a % pair)
        for a in range(across)
        for b in range(across)
    ]
    near = lax.ppermute(tokens, ("x",) + SUB, swap)
    far = lax.ppermute(tokens, ("x",) + SUB, cross)
    both = jnp.stack([jnp.where(me_h == 0, near, far), jnp.where(me_h == 0, far, near)])
    gathered = lax.all_gather(both, ("y", "c"), axis=0, tiled=False)
    blocks = gathered.reshape(-1, pair, halves, tok_rows, feat_block)

    def contribution(source, weight):
        taken = lax.dynamic_index_in_dim(blocks, source, axis=0, keepdims=False)
        return jnp.einsum("chru,uk->hcrk", taken, weight, preferred_element_type=jnp.float32)

    reduced = {}
    for s in order:
        below, above = relays[s]
        partial = contribution(me_z, in_weight[:, s, :])
        for d in range(1, down):
            low, high = jnp.maximum(me_z - d, 0), jnp.minimum(me_z + d, down - 1)
            if 2 * d <= down - 1:
                partial = partial + contribution(low, below[d - 1])
                partial = partial + contribution(high, above[d - 1])
            else:
                use_low = me_z - d >= 0
                weight = jnp.where(use_low, below[d - 1], above[d - 1])
                partial = partial + contribution(jnp.where(use_low, low, high), weight)
        partial = partial.reshape(across, tok_rows, width_local)
        total = lax.dynamic_index_in_dim(partial, me_x, axis=0, keepdims=False)
        for k in sorted(range(1, across), key=lambda k: -min(k, across - k)):
            route = [(i, (i + k) % across) for i in range(across)]
            piece = lax.dynamic_index_in_dim(partial, (me_x + k) % across, axis=0, keepdims=False)
            total = total + lax.ppermute(piece, "x", route)
        reduced[s] = total
    tap_count = short_filter.shape[0]
    filter_taps = short_filter.astype(jnp.float32)

    def short_conv(group):
        streams = jnp.stack([reduced[t] for t in group], axis=1).astype(jnp.bfloat16)
        last_rows = streams[tok_rows - (tap_count - 1) :]
        before = from_behind(last_rows, SEQ, 1)
        padded = jnp.concatenate([before, streams], axis=0).astype(jnp.float32)
        taps = filter_taps[:, group[0] : group[-1] + 1]
        featured = jnp.zeros((tok_rows, len(group), width_local), jnp.float32)
        for shift_back in range(tap_count):
            begin = tap_count - 1 - shift_back
            featured = featured + taps[shift_back][None] * padded[begin : begin + tok_rows]
        return featured

    gates = short_conv(order[:-1])
    gated_rows = (gates[:, 0] * gates[:, 1]).astype(jnp.bfloat16)
    gated_wide = gated_rows.astype(jnp.float32)
    position = jnp.arange(tok_rows, dtype=jnp.float32)
    powers = jnp.exp(-decay_rate[None, :, :] * (tok_rows - 1.0 - position)[:, None, None])
    local_state = jnp.einsum("jc,jcr->cr", gated_wide, powers, precision=exact_mode)
    along = [local_state] + ring_sends(lambda k, p: local_state, "x", across)
    row = jnp.stack(along)
    states = jnp.stack([row] + ring_sends(lambda k, p: row, "zl", down))
    step_z = jnp.arange(down)[:, None]
    step_x = jnp.arange(across)[None, :]
    source = ((me_z - step_z) % down) * across + (me_x - step_x) % across
    lag = (me_z * across + me_x - 1 - source).astype(jnp.float32)
    decay_b = decay_rate[None, None]
    weight = jnp.exp(-decay_b * (float(tok_rows) * jnp.maximum(lag, 0.0))[:, :, None, None])
    weight = jnp.where((lag >= 0)[:, :, None, None], weight, 0.0)
    incoming = jnp.sum(weight * states, axis=(0, 1))
    growth = jnp.exp(decay_rate[None, :, :] * position[:, None, None])
    scaled = (gated_wide[:, :, None] * growth).reshape(tok_rows, width_local * mode_count)
    lower_mask = (jnp.arange(tok_rows)[:, None] >= jnp.arange(tok_rows)[None, :]).astype(
        jnp.float32
    )
    running_sum = jnp.dot(lower_mask, scaled, precision=exact_mode).reshape(
        tok_rows, width_local, mode_count
    )
    shrink = jnp.exp(-decay_rate[None, :, :] * position[:, None, None])
    entering = (incoming * jnp.exp(-decay_rate))[None]
    convolved = jnp.sum(residue[None] * shrink * (running_sum + entering), axis=2)
    long_mix = convolved + skip_gain[None, :] * gated_wide
    query_gate = short_conv(order[-1:])[:, 0]
    return (query_gate * long_mix).astype(jnp.bfloat16)


def split_mesh(mesh):
    ctx, ch = mesh.shape["ctx"], mesh.shape["ch"]
    devices = np.asarray(mesh.devices).reshape(ctx // 4, 4, ch // 4, 2, 2)
    return Mesh(devices, SEQ + CH)


def solution(mesh):
    fine = split_mesh(mesh)
    in_specs = (
        P(SEQ, CH),
        P(SEQ, None, CH),
        P(None, None, CH),
        P(CH, None),
        P(CH, None),
        P(CH),
    )
    out_specs = P(SEQ, CH)
    return jax.shard_map(block, mesh=fine, in_specs=in_specs, out_specs=out_specs, check_vma=False)
```
